32 devices in a mesh: pair: 8 (over z, core), orb: 4 (over y, x).
Axes of the slice: x: 2, y: 2, z: 4, core: 2. Of those that a mesh axis runs over, the one named last changes fastest.
Arguments:
- amplitudes: bfloat16 [8, 2, 600, 600], P('pair', None, 'orb'), may hold values from -6 to 6
- factors: bfloat16 [48, 360000], P('orb', 'pair'), may hold values from -0.21875 to 0.21875
- crossed_amplitudes: bfloat16 [8, 64, 600, 600], P('pair', None, 'orb'), may hold values from -6 to 6
- crossed_coupling: bfloat16 [38400, 1200], P('orb', 'pair'), may hold values from -0.03125 to 0.03125
Outputs:
- residual: float32 [8, 600, 2, 600], P('pair', 'orb')
The draws below stay inside these ranges and needn't reach their ends.
All inputs are finite; a program needn't handle non-finite values.
Results may differ from the reference program's by a relative error of at most 0.0023.
Values may be sent and summed in bfloat16 or wider, within the bound.
No kernel may reach another device: no remote copies, remote signals or barrier semaphores. Data moves between devices by JAX's collectives and lax.ppermute only.
A program may use at most 256 MiB of HBM per device.

```python
import jax
import jax.numpy as jnp
from jax import lax

NV = 600
KOCC = 64
NJ = 2
NI = 8
NQ = 48


def steps_of(key, extent, cuts, low, top_value):
    loudness, own = 1.0, jax.random.fold_in(key, 6)
    for axis_at, parts in cuts:
        draws = jnp.exp(jax.random.uniform(jax.random.fold_in(own, axis_at), (parts,), jnp.float32, low / len(cuts), top_value / len(cuts)))
        loudness = loudness * jnp.repeat(draws, extent[axis_at] // parts).reshape([-1 if axis == axis_at else 1 for axis in range(len(extent))])
    return loudness


def normal_values(stream_key, shape, width, bound, pieces=(), held_as=jnp.bfloat16):
    loudness = steps_of(stream_key, shape, pieces, -0.22, 0.18) if pieces else 1.0
    array = jax.random.normal(stream_key, shape, jnp.float32) * width * loudness
    return jnp.minimum(jnp.maximum(array, -bound), bound).astype(held_as)


def setup_inputs(seed: int = 0) -> dict:
    splits = jax.random.split(jax.random.key(seed), 5)
    amplitudes = normal_values(splits[0], (NI, NJ, NV, NV), 1.0, 6.0, ((0, 8), (2, 4)))
    factors = normal_values(splits[1], (NQ, NV * NV), ((NQ * NV * NV) ** -0.25), 0.21875, ((0, 4), (1, 8)))
    crossed_amplitudes = normal_values(splits[2], (NI, KOCC, NV, NV), 1.0, 6.0, ((0, 8), (2, 4)))
    crossed_coupling = normal_values(splits[3], (KOCC * NV, NJ * NV), (KOCC * NV) ** -0.5, 0.03125, ((0, 4), (1, 8)))
    return dict(amplitudes=amplitudes, factors=factors, crossed_amplitudes=crossed_amplitudes, crossed_coupling=crossed_coupling)


def reference(amplitudes, factors, crossed_amplitudes, crossed_coupling):
    cube = factors.reshape(NQ, NV, NV).astype(jnp.float32)

    def ladder_pair(pair_amp):
        inner = jnp.einsum("qac,cd->qad", cube, pair_amp.astype(jnp.float32))
        inner = lax.optimization_barrier(inner.astype(jnp.bfloat16)).astype(jnp.float32)
        return jnp.einsum("qad,qbd->ab", inner, cube)

    ladder = lax.map(ladder_pair, amplitudes.reshape(NI * NJ, NV, NV))
    ladder = ladder.reshape(NI, NJ, NV, NV).transpose(0, 2, 1, 3)
    coupling = crossed_coupling.astype(jnp.float32).reshape(KOCC, NV, NJ * NV)

    def crossed_row(row_amp):
        return jnp.einsum("kac,kcn->an", row_amp.astype(jnp.float32), coupling)

    crossed = lax.map(crossed_row, crossed_amplitudes).reshape(NI, NV, NJ, NV)
    return ladder + crossed
```

```python
import jax
import jax.numpy as jnp
from jax import lax
from jax.sharding import Mesh, PartitionSpec as P

NV = 600
PAIR = ("zz", "core")


def pair_gather(x):
    g = lax.all_gather(x, "zz", axis=0, tiled=False)
    g = lax.all_gather(g, "core", axis=1, tiled=False)
    return g.reshape((g.shape[0] * g.shape[1],) + x.shape)


def ladder_term(amplitudes, factors, nvirt):
    nj = amplitudes.shape[1]
    t = lax.all_gather(amplitudes[0], "orb", axis=0, tiled=False)
    tm = t.transpose(0, 2, 1, 3).reshape(nvirt, nj * nvirt)
    g = pair_gather(factors)
    nq = factors.shape[0]
    cube = g.transpose(1, 0, 2).reshape(nq, nvirt, nvirt)
    inner = jnp.einsum("qac,cn->qan", cube, tm, preferred_element_type=jnp.float32).astype(jnp.bfloat16)
    inner = inner.reshape(nq, nvirt, nj, nvirt)
    return jnp.einsum("qajd,qbd->ajb", inner, cube, preferred_element_type=jnp.float32)


def crossed_term(crossed_amplitudes, crossed_coupling, nvirt, norb):
    ca = crossed_amplitudes[0]
    kocc, nva = ca.shape[0], ca.shape[1]
    kl = kocc // norb
    ca = ca.reshape(norb, kl, nva, nvirt)
    r = lax.all_to_all(ca, "orb", 0, 0, tiled=True)
    lhs = r.transpose(0, 2, 1, 3).reshape(norb * nva, kl * nvirt)
    w = pair_gather(crossed_coupling)
    product = jnp.einsum("ak,pkc->apc", lhs, w, preferred_element_type=jnp.float32)
    return product.reshape(nvirt, -1, nvirt)


def on_device(amplitudes, factors, crossed_amplitudes, crossed_coupling):
    nvirt = NV
    norb = lax.axis_size("orb")
    ladder = ladder_term(amplitudes, factors, nvirt)
    crossed = crossed_term(crossed_amplitudes, crossed_coupling, nvirt, norb)
    total = (ladder + crossed).reshape((norb, nvirt // norb) + ladder.shape[1:])
    total = lax.psum_scatter(total, "orb", scatter_dimension=0, tiled=True)
    return total


def solution(mesh):
    npair, norb = mesh.shape["pair"], mesh.shape["orb"]
    sub = Mesh(mesh.devices.reshape(npair // 2, 2, norb), ("zz", "core", "orb"))
    return jax.shard_map(
        on_device,
        mesh=sub,
        in_specs=(
            P(PAIR, None, "orb", None),
            P("orb", PAIR),
            P(PAIR, None, "orb", None),
            P("orb", PAIR),
        ),
        out_specs=P(PAIR, "orb", None, None),
        check_vma=False,
    )
```

```python
import jax
import jax.numpy as jnp
from jax import lax
from jax.sharding import Mesh, PartitionSpec as P

NV = 600
PAIR = ("zz", "core")


def relay(x, n):
    zz = lax.axis_index("zz")
    out = [(x, zz)]
    right, left = x, x
    for s in range(1, n):
        right = lax.ppermute(right, "zz", [(i, i + 1) for i in range(s - 1, n - 1)])
        left = lax.ppermute(left, "zz", [(j, j - 1) for j in range(1, n - s + 1)])
        out.append((right, jnp.maximum(zz - s, 0)))
        out.append((left, jnp.minimum(zz + s, n - 1)))
    return out


def ladder_term(amplitudes, factors, nvirt):
    nj = amplitudes.shape[1]
    t = lax.all_gather(amplitudes[0], "orb", axis=0, tiled=False)
    tm = t.transpose(0, 2, 1, 3).reshape(nvirt, nj * nvirt)
    g = lax.all_gather(factors, PAIR, axis=0, tiled=False)
    nq = factors.shape[0]
    cube = g.transpose(1, 0, 2).reshape(nq, nvirt, nvirt)
    inner = jnp.einsum("qac,cn->qan", cube, tm, preferred_element_type=jnp.float32).astype(jnp.bfloat16)
    inner = inner.reshape(nq, nvirt, nj, nvirt)
    return jnp.einsum("qajd,qbd->ajb", inner, cube, preferred_element_type=jnp.float32)


def crossed_term(crossed_amplitudes, crossed_coupling, nvirt, norb, nchip):
    ca = crossed_amplitudes[0]
    kocc, nva = ca.shape[0], ca.shape[1]
    kl = kocc // norb
    ca = ca.reshape(norb, kl, nva, nvirt)
    r = lax.all_to_all(ca, "orb", 0, 0, tiled=True)
    lhs = r.transpose(0, 2, 1, 3).reshape(norb * nva, kl * nvirt)
    wt = crossed_coupling.T
    ncol = wt.shape[0]
    core = lax.axis_index("core")
    out = jnp.zeros((lhs.shape[0], 2 * nchip, ncol), jnp.float32)
    for block, origin in relay(wt, nchip):
        other = lax.ppermute(block, "core", [(0, 1), (1, 0)])
        for b, c in ((block, core), (other, 1 - core)):
            part = jnp.einsum("ak,nk->an", lhs, b, preferred_element_type=jnp.float32)
            at = 2 * origin + c
            cur = lax.dynamic_slice_in_dim(out, at, 1, axis=1)
            out = lax.dynamic_update_slice_in_dim(out, cur + part[:, None], at, axis=1)
    return out.reshape(nvirt, -1, nvirt)


def on_device(amplitudes, factors, crossed_amplitudes, crossed_coupling):
    nvirt = NV
    norb = lax.axis_size("orb")
    nchip = lax.axis_size("zz")
    ladder = ladder_term(amplitudes, factors, nvirt)
    crossed = crossed_term(crossed_amplitudes, crossed_coupling, nvirt, norb, nchip)
    total = (ladder + crossed).reshape((norb, nvirt // norb) + ladder.shape[1:])
    return lax.psum_scatter(total, "orb", scatter_dimension=0, tiled=True)


def solution(mesh):
    npair, norb = mesh.shape["pair"], mesh.shape["orb"]
    sub = Mesh(mesh.devices.reshape(npair // 2, 2, norb), ("zz", "core", "orb"))
    return jax.shard_map(
        on_device,
        mesh=sub,
        in_specs=(
            P(PAIR, None, "orb", None),
            P("orb", PAIR),
            P(PAIR, None, "orb", None),
            P("orb", PAIR),
        ),
        out_specs=P(PAIR, "orb", None, None),
        check_vma=False,
    )
```

```python
import jax
import jax.numpy as jnp
from jax import lax
from jax.sharding import Mesh, PartitionSpec as P

NV = 600
PAIR = ("zz", "core")


def relay(x, n):
    zz = lax.axis_index("zz")
    out = [(x, zz)]
    right, left = x, x
    for s in range(1, n):
        right = lax.ppermute(right, "zz", [(i, i + 1) for i in range(s - 1, n - 1)])
        left = lax.ppermute(left, "zz", [(j, j - 1) for j in range(1, n - s + 1)])
        out.append((right, jnp.maximum(zz - s, 0)))
        out.append((left, jnp.minimum(zz + s, n - 1)))
    return out


def ladder_term(amplitudes, factors, nvirt):
    nj = amplitudes.shape[1]
    t = lax.all_gather(amplitudes[0], "orb", axis=0, tiled=False)
    nq, cols = factors.shape
    if cols % nvirt == 0:
        g = lax.all_gather(factors.reshape(nq, cols // nvirt, nvirt), PAIR, axis=0, tiled=False)
        cube = None
    else:
        g = lax.all_gather(factors, PAIR, axis=0, tiled=False)
        cube = g.transpose(1, 0, 2).reshape(nq, nvirt, nvirt)
    parts = []
    for j in range(nj):
        tj = t[:, j].reshape(nvirt, nvirt)
        if cube is None:
            inner = jnp.einsum("pqac,cd->pqad", g, tj, preferred_element_type=jnp.float32).astype(jnp.bfloat16)
            lj = jnp.einsum("pqad,rqbd->parb", inner, g, preferred_element_type=jnp.float32)
        else:
            inner = jnp.einsum("qac,cd->qad", cube, tj, preferred_element_type=jnp.float32).astype(jnp.bfloat16)
            lj = jnp.einsum("qad,qbd->ab", inner, cube, preferred_element_type=jnp.float32)
        parts.append(lj.reshape(nvirt, nvirt))
    return jnp.stack(parts, axis=1)


def crossed_term(crossed_amplitudes, crossed_coupling, nvirt, norb, nchip):
    ca = crossed_amplitudes[0]
    kocc, nva = ca.shape[0], ca.shape[1]
    kl = kocc // norb
    ca = ca.reshape(norb, kl, nva, nvirt)
    r = lax.all_to_all(ca, "orb", 0, 0, tiled=True)
    lhs = r.transpose(0, 2, 1, 3).reshape(norb * nva, kl * nvirt)
    wt = crossed_coupling.T
    ncol = wt.shape[0]
    core = lax.axis_index("core")
    out = jnp.zeros((lhs.shape[0], 2 * nchip, ncol), jnp.float32)
    for block, origin in relay(wt, nchip):
        other = lax.ppermute(block, "core", [(0, 1), (1, 0)])
        for b, c in ((block, core), (other, 1 - core)):
            part = jnp.einsum("ak,nk->an", lhs, b, preferred_element_type=jnp.float32)
            at = 2 * origin + c
            cur = lax.dynamic_slice_in_dim(out, at, 1, axis=1)
            out = lax.dynamic_update_slice_in_dim(out, cur + part[:, None], at, axis=1)
    return out.reshape(nvirt, -1, nvirt)


def on_device(amplitudes, factors, crossed_amplitudes, crossed_coupling):
    nvirt = NV
    norb = lax.axis_size("orb")
    nchip = lax.axis_size("zz")
    ladder = ladder_term(amplitudes, factors, nvirt)
    crossed = crossed_term(crossed_amplitudes, crossed_coupling, nvirt, norb, nchip)
    total = (ladder + crossed).reshape((norb, nvirt // norb) + ladder.shape[1:])
    return reduce_scatter(total, norb)[None]


def reduce_scatter(total, norb):
    me = lax.axis_index("orb")
    acc = lax.dynamic_index_in_dim(total, me, axis=0, keepdims=False)
    pow2 = norb & (norb - 1) == 0
    for s in range(1, norb):
        if pow2:
            pairs = [(o, o ^ s) for o in range(norb)]
            dest = jnp.bitwise_xor(me, s)
        else:
            pairs = [(o, (o + s) % norb) for o in range(norb)]
            dest = (me + s) % norb
        blk = lax.dynamic_index_in_dim(total, dest, axis=0, keepdims=False)
        acc = acc + lax.ppermute(blk, "orb", pairs)
    return acc


def solution(mesh):
    npair, norb = mesh.shape["pair"], mesh.shape["orb"]
    sub = Mesh(mesh.devices.reshape(npair // 2, 2, norb), ("zz", "core", "orb"))
    return jax.shard_map(
        on_device,
        mesh=sub,
        in_specs=(
            P(PAIR, None, "orb", None),
            P("orb", PAIR),
            P(PAIR, None, "orb", None),
            P("orb", PAIR),
        ),
        out_specs=P(PAIR, "orb", None, None),
        check_vma=False,
    )
```

```python
import jax
import jax.numpy as jnp
from jax import lax
from jax.sharding import Mesh, PartitionSpec as P

NV = 600
PAIR = ("zz", "core")


def relay(x, n):
    zz = lax.axis_index("zz")
    out = [(x, zz)]
    right, left = x, x
    for s in range(1, n):
        right = lax.ppermute(right, "zz", [(i, i + 1) for i in range(s - 1, n - 1)])
        left = lax.ppermute(left, "zz", [(j, j - 1) for j in range(1, n - s + 1)])
        out.append((right, jnp.maximum(zz - s, 0)))
        out.append((left, jnp.minimum(zz + s, n - 1)))
    return out


def ladder_term(amplitudes, factors, nvirt):
    nj = amplitudes.shape[1]
    t = lax.all_gather(amplitudes[0], "orb", axis=0, tiled=False)
    nq, cols = factors.shape
    if cols % nvirt == 0:
        g = lax.all_gather(factors.reshape(nq, cols // nvirt, nvirt), PAIR, axis=0, tiled=False)
        cube = None
    else:
        g = lax.all_gather(factors, PAIR, axis=0, tiled=False)
        cube = g.transpose(1, 0, 2).reshape(nq, nvirt, nvirt)
    return ladder_math(t, g, cube, nj, nvirt)


def ladder_math(t, g, cube, nj, nvirt):
    parts = []
    for j in range(nj):
        tj = t[:, j].reshape(nvirt, nvirt)
        if cube is None:
            inner = jnp.einsum("pqac,cd->pqad", g, tj, preferred_element_type=jnp.float32).astype(jnp.bfloat16)
            lj = jnp.einsum("pqad,rqbd->parb", inner, g, preferred_element_type=jnp.float32)
        else:
            inner = jnp.einsum("qac,cd->qad", cube, tj, preferred_element_type=jnp.float32).astype(jnp.bfloat16)
            lj = jnp.einsum("qad,qbd->ab", inner, cube, preferred_element_type=jnp.float32)
        parts.append(lj.reshape(nvirt, nvirt))
    return jnp.stack(parts, axis=1)


def crossed_term(crossed_amplitudes, crossed_coupling, nvirt, norb, nchip):
    ca = crossed_amplitudes[0]
    kocc, nva = ca.shape[0], ca.shape[1]
    kl = kocc // norb
    ca = ca.reshape(norb, kl, nva, nvirt)
    r = lax.all_to_all(ca, "orb", 0, 0, tiled=True)
    lhs = r.transpose(0, 2, 1, 3).reshape(norb * nva, kl * nvirt)
    wt = crossed_coupling.T
    ncol = wt.shape[0]
    core = lax.axis_index("core")
    out = jnp.zeros((lhs.shape[0], 2 * nchip, ncol), jnp.float32)
    for block, origin in relay(wt, nchip):
        other = lax.ppermute(block, "core", [(0, 1), (1, 0)])
        for b, c in ((block, core), (other, 1 - core)):
            part = jnp.einsum("ak,nk->an", lhs, b, preferred_element_type=jnp.float32)
            at = 2 * origin + c
            cur = lax.dynamic_slice_in_dim(out, at, 1, axis=1)
            out = lax.dynamic_update_slice_in_dim(out, cur + part[:, None], at, axis=1)
    return out.reshape(nvirt, -1, nvirt)


def on_device_body(amplitudes, factors, crossed_amplitudes, crossed_coupling):
    nvirt = NV
    norb = lax.axis_size("orb")
    nchip = lax.axis_size("zz")
    ladder = ladder_term(amplitudes, factors, nvirt)
    crossed = crossed_term(crossed_amplitudes, crossed_coupling, nvirt, norb, nchip)
    total = (ladder + crossed).reshape((norb, nvirt // norb) + ladder.shape[1:])
    return reduce_scatter(total, norb)[None]


def reduce_scatter(total, norb):
    me = lax.axis_index("orb")
    acc = lax.dynamic_index_in_dim(total, me, axis=0, keepdims=False)
    pow2 = norb & (norb - 1) == 0
    for s in range(1, norb):
        if pow2:
            pairs = [(o, o ^ s) for o in range(norb)]
            dest = jnp.bitwise_xor(me, s)
        else:
            pairs = [(o, (o + s) % norb) for o in range(norb)]
            dest = (me + s) % norb
        blk = lax.dynamic_index_in_dim(total, dest, axis=0, keepdims=False)
        acc = acc + lax.ppermute(blk, "orb", pairs)
    return acc


def solution(mesh):
    npair, norb = mesh.shape["pair"], mesh.shape["orb"]
    sub = Mesh(mesh.devices.reshape(npair // 2, 2, norb), ("zz", "core", "orb"))
    return jax.shard_map(
        on_device_body,
        mesh=sub,
        in_specs=(
            P(PAIR, None, "orb", None),
            P("orb", PAIR),
            P(PAIR, None, "orb", None),
            P("orb", PAIR),
        ),
        out_specs=P(PAIR, "orb", None, None),
        check_vma=False,
    )
```

```python
import jax
import jax.numpy as jnp
from jax import lax
from jax.sharding import Mesh, PartitionSpec as P

NV = 600
PAIR = ("zz", "core")


def relay(x, n):
    zz = lax.axis_index("zz")
    out = [(x, zz, zz >= 0)]
    right, left = x, x
    for s in range(1, n):
        right = lax.ppermute(right, "zz", [(i, i + 1) for i in range(s - 1, n - 1)])
        left = lax.ppermute(left, "zz", [(j, j - 1) for j in range(1, n - s + 1)])
        out.append((right, jnp.maximum(zz - s, 0), zz - s >= 0))
        out.append((left, jnp.minimum(zz + s, n - 1), zz + s <= n - 1))
    return out


def relay_gather(x, n):
    core = lax.axis_index("core")
    buf = jnp.zeros((2 * n + 1,) + x.shape, x.dtype)
    for block, origin, valid in relay(x, n):
        other = lax.ppermute(block, "core", [(0, 1), (1, 0)])
        for b, c in ((block, core), (other, 1 - core)):
            at = jnp.where(valid, 2 * origin + c, 2 * n)
            buf = lax.dynamic_update_index_in_dim(buf, b, at, axis=0)
    return buf[: 2 * n]


def ladder_term(amplitudes, factors, nvirt):
    nj = amplitudes.shape[1]
    t = lax.all_gather(amplitudes[0], "orb", axis=0, tiled=False)
    nq, cols = factors.shape
    if cols % nvirt == 0:
        g = relay_gather(factors.reshape(nq, cols // nvirt, nvirt), lax.axis_size("zz"))
        cube = None
    else:
        g = lax.all_gather(factors, PAIR, axis=0, tiled=False)
        cube = g.transpose(1, 0, 2).reshape(nq, nvirt, nvirt)
    return ladder_math(t, g, cube, nj, nvirt)


def ladder_math(t, g, cube, nj, nvirt):
    parts = []
    for j in range(nj):
        tj = t[:, j].reshape(nvirt, nvirt)
        if cube is None:
            inner = jnp.einsum("pqac,cd->pqad", g, tj, preferred_element_type=jnp.float32).astype(jnp.bfloat16)
            lj = jnp.einsum("pqad,rqbd->parb", inner, g, preferred_element_type=jnp.float32)
        else:
            inner = jnp.einsum("qac,cd->qad", cube, tj, preferred_element_type=jnp.float32).astype(jnp.bfloat16)
            lj = jnp.einsum("qad,qbd->ab", inner, cube, preferred_element_type=jnp.float32)
        parts.append(lj.reshape(nvirt, nvirt))
    return jnp.stack(parts, axis=1)


def crossed_term(crossed_amplitudes, crossed_coupling, nvirt, norb, nchip):
    ca = crossed_amplitudes[0]
    kocc, nva = ca.shape[0], ca.shape[1]
    kl = kocc // norb
    ca = ca.reshape(norb, kl, nva, nvirt)
    r = lax.all_to_all(ca, "orb", 0, 0, tiled=True)
    lhs = r.transpose(0, 2, 1, 3).reshape(norb * nva, kl * nvirt)
    wt = crossed_coupling.T
    ncol = wt.shape[0]
    core = lax.axis_index("core")
    out = jnp.zeros((lhs.shape[0], 2 * nchip, ncol), jnp.float32)
    for block, origin, _ in relay(wt, nchip):
        other = lax.ppermute(block, "core", [(0, 1), (1, 0)])
        for b, c in ((block, core), (other, 1 - core)):
            part = jnp.einsum("ak,nk->an", lhs, b, preferred_element_type=jnp.float32)
            at = 2 * origin + c
            cur = lax.dynamic_slice_in_dim(out, at, 1, axis=1)
            out = lax.dynamic_update_slice_in_dim(out, cur + part[:, None], at, axis=1)
    return out.reshape(nvirt, -1, nvirt)


def on_device_body(amplitudes, factors, crossed_amplitudes, crossed_coupling):
    nvirt = NV
    norb = lax.axis_size("orb")
    nchip = lax.axis_size("zz")
    ladder = ladder_term(amplitudes, factors, nvirt)
    crossed = crossed_term(crossed_amplitudes, crossed_coupling, nvirt, norb, nchip)
    total = (ladder + crossed).reshape((norb, nvirt // norb) + ladder.shape[1:])
    return reduce_scatter(total, norb)[None]


def reduce_scatter(total, norb):
    me = lax.axis_index("orb")
    acc = lax.dynamic_index_in_dim(total, me, axis=0, keepdims=False)
    pow2 = norb & (norb - 1) == 0
    for s in range(1, norb):
        if pow2:
            pairs = [(o, o ^ s) for o in range(norb)]
            dest = jnp.bitwise_xor(me, s)
        else:
            pairs = [(o, (o + s) % norb) for o in range(norb)]
            dest = (me + s) % norb
        blk = lax.dynamic_index_in_dim(total, dest, axis=0, keepdims=False)
        acc = acc + lax.ppermute(blk, "orb", pairs)
    return acc


def solution(mesh):
    npair, norb = mesh.shape["pair"], mesh.shape["orb"]
    sub = Mesh(mesh.devices.reshape(npair // 2, 2, norb), ("zz", "core", "orb"))
    return jax.shard_map(
        on_device_body,
        mesh=sub,
        in_specs=(
            P(PAIR, None, "orb", None),
            P("orb", PAIR),
            P(PAIR, None, "orb", None),
            P("orb", PAIR),
        ),
        out_specs=P(PAIR, "orb", None, None),
        check_vma=False,
    )
```

```python
import jax
import jax.numpy as jnp
from jax import lax
from jax.sharding import Mesh, PartitionSpec as P

NV = 600
PAIR = ("zz", "core")


def relay(x, n):
    zz = lax.axis_index("zz")
    out = [(x, zz, zz >= 0)]
    right, left = x, x
    for s in range(1, n):
        right = lax.ppermute(right, "zz", [(i, i + 1) for i in range(s - 1, n - 1)])
        left = lax.ppermute(left, "zz", [(j, j - 1) for j in range(1, n - s + 1)])
        out.append((right, jnp.maximum(zz - s, 0), zz - s >= 0))
        out.append((left, jnp.minimum(zz + s, n - 1), zz + s <= n - 1))
    return out


def relay_gather(x, n):
    core = lax.axis_index("core")
    buf = jnp.zeros((2 * n + 1,) + x.shape, x.dtype)
    for block, origin, valid in relay(x, n):
        other = lax.ppermute(block, "core", [(0, 1), (1, 0)])
        for b, c in ((block, core), (other, 1 - core)):
            at = jnp.where(valid, 2 * origin + c, 2 * n)
            buf = lax.dynamic_update_index_in_dim(buf, b, at, axis=0)
    return buf[: 2 * n]


def ladder_term(t, factors, nvirt):
    nj = t.shape[1]
    nq, cols = factors.shape
    if cols % nvirt == 0:
        g = relay_gather(factors.reshape(nq, cols // nvirt, nvirt), lax.axis_size("zz"))
        cube = None
    else:
        g = lax.all_gather(factors, PAIR, axis=0, tiled=False)
        cube = g.transpose(1, 0, 2).reshape(nq, nvirt, nvirt)
    return ladder_math(t, g, cube, nj, nvirt)


def ladder_math(t, g, cube, nj, nvirt):
    parts = []
    for j in range(nj):
        tj = t[:, j].reshape(nvirt, nvirt)
        if cube is None:
            inner = jnp.einsum("pqac,cd->pqad", g, tj, preferred_element_type=jnp.float32).astype(jnp.bfloat16)
            lj = jnp.einsum("pqad,rqbd->parb", inner, g, preferred_element_type=jnp.float32)
        else:
            inner = jnp.einsum("qac,cd->qad", cube, tj, preferred_element_type=jnp.float32).astype(jnp.bfloat16)
            lj = jnp.einsum("qad,qbd->ab", inner, cube, preferred_element_type=jnp.float32)
        parts.append(lj.reshape(nvirt, nvirt))
    return jnp.stack(parts, axis=1)


def crossed_term(crossed_amplitudes, crossed_coupling, nvirt, norb, nchip):
    ca = crossed_amplitudes[0]
    kocc, nva = ca.shape[0], ca.shape[1]
    kl = kocc // norb
    ca = ca.reshape(norb, kl, nva, nvirt)
    r = lax.all_to_all(ca, "orb", 0, 0, tiled=True)
    lhs = r.transpose(0, 2, 1, 3).reshape(norb * nva, kl * nvirt)
    wt = crossed_coupling.T
    ncol = wt.shape[0]
    core = lax.axis_index("core")
    out = jnp.zeros((nva, 2 * nchip, ncol), jnp.float32)
    entries = relay(wt, nchip)
    groups = [entries[:1]] + [entries[i:i + 2] for i in range(1, len(entries), 2)]
    for group in groups:
        blocks, places = [], []
        for block, origin, _ in group:
            other = lax.ppermute(block, "core", [(0, 1), (1, 0)])
            for b, c in ((block, core), (other, 1 - core)):
                blocks.append(jnp.einsum("ak,nk->an", lhs, b, preferred_element_type=jnp.float32))
                places.append(2 * origin + c)
        part = jnp.stack(blocks, axis=1)
        part = reduce_scatter(part.reshape((norb, nva) + part.shape[1:]), norb)
        for i, at in enumerate(places):
            cur = lax.dynamic_slice_in_dim(out, at, 1, axis=1)
            out = lax.dynamic_update_slice_in_dim(out, cur + part[:, i : i + 1], at, axis=1)
    return out.reshape(nva, -1, nvirt)


def on_device_body(amplitudes, factors, crossed_amplitudes, crossed_coupling):
    nvirt = NV
    norb = lax.axis_size("orb")
    nchip = lax.axis_size("zz")
    t = lax.all_gather(amplitudes[0], "orb", axis=0, tiled=False)
    t, crossed_amplitudes = lax.optimization_barrier((t, crossed_amplitudes))
    ladder = ladder_term(t, factors, nvirt)
    ladder = reduce_scatter(ladder.reshape((norb, nvirt // norb) + ladder.shape[1:]), norb)
    crossed = crossed_term(crossed_amplitudes, crossed_coupling, nvirt, norb, nchip)
    return (ladder + crossed)[None]


def reduce_scatter(total, norb):
    me = lax.axis_index("orb")
    acc = lax.dynamic_index_in_dim(total, me, axis=0, keepdims=False)
    pow2 = norb & (norb - 1) == 0
    for s in range(1, norb):
        if pow2:
            pairs = [(o, o ^ s) for o in range(norb)]
            dest = jnp.bitwise_xor(me, s)
        else:
            pairs = [(o, (o + s) % norb) for o in range(norb)]
            dest = (me + s) % norb
        blk = lax.dynamic_index_in_dim(total, dest, axis=0, keepdims=False)
        acc = acc + lax.ppermute(blk, "orb", pairs)
    return acc


def solution(mesh):
    npair, norb = mesh.shape["pair"], mesh.shape["orb"]
    sub = Mesh(mesh.devices.reshape(npair // 2, 2, norb), ("zz", "core", "orb"))
    return jax.shard_map(
        on_device_body,
        mesh=sub,
        in_specs=(
            P(PAIR, None, "orb", None),
            P("orb", PAIR),
            P(PAIR, None, "orb", None),
            P("orb", PAIR),
        ),
        out_specs=P(PAIR, "orb", None, None),
        check_vma=False,
    )
```

```python
import jax
import jax.numpy as jnp
from jax import lax
from jax.sharding import Mesh, PartitionSpec as P

NV = 600
PAIR = ("zz", "core")


def relay(x, n):
    zz = lax.axis_index("zz")
    out = [(x, zz, zz >= 0)]
    right, left = x, x
    for s in range(1, n):
        right = lax.ppermute(right, "zz", [(i, i + 1) for i in range(s - 1, n - 1)])
        left = lax.ppermute(left, "zz", [(j, j - 1) for j in range(1, n - s + 1)])
        out.append((right, jnp.maximum(zz - s, 0), zz - s >= 0))
        out.append((left, jnp.minimum(zz + s, n - 1), zz + s <= n - 1))
    return out


def relay_gather(x, n):
    core = lax.axis_index("core")
    buf = jnp.zeros((2 * n + 1,) + x.shape, x.dtype)
    for block, origin, valid in relay(x, n):
        other = lax.ppermute(block, "core", [(0, 1), (1, 0)])
        for b, c in ((block, core), (other, 1 - core)):
            at = jnp.where(valid, 2 * origin + c, 2 * n)
            buf = lax.dynamic_update_index_in_dim(buf, b, at, axis=0)
    return buf[: 2 * n]


def ladder_term(t, factors, nvirt):
    nj = t.shape[1]
    nq, cols = factors.shape
    if cols % nvirt == 0:
        g = relay_gather(factors.reshape(nq, cols // nvirt, nvirt), lax.axis_size("zz"))
        cube = None
    else:
        g = lax.all_gather(factors, PAIR, axis=0, tiled=False)
        cube = g.transpose(1, 0, 2).reshape(nq, nvirt, nvirt)
    return ladder_math(t, g, cube, nj, nvirt)


def ladder_math(t, g, cube, nj, nvirt):
    parts = []
    for j in range(nj):
        tj = t[:, j].reshape(nvirt, nvirt)
        if cube is None:
            inner = jnp.einsum("pqac,cd->pqad", g, tj, preferred_element_type=jnp.float32).astype(jnp.bfloat16)
            lj = jnp.einsum("pqad,rqbd->parb", inner, g, preferred_element_type=jnp.float32)
        else:
            inner = jnp.einsum("qac,cd->qad", cube, tj, preferred_element_type=jnp.float32).astype(jnp.bfloat16)
            lj = jnp.einsum("qad,qbd->ab", inner, cube, preferred_element_type=jnp.float32)
        parts.append(lj.reshape(nvirt, nvirt))
    return jnp.stack(parts, axis=1)


def crossed_term(crossed_amplitudes, crossed_coupling, nvirt, norb, nchip):
    ca = crossed_amplitudes[0]
    kocc, nva = ca.shape[0], ca.shape[1]
    kl = kocc // norb
    ca = ca.reshape(norb, kl, nva, nvirt)
    r = lax.all_to_all(ca, "orb", 0, 0, tiled=True)
    lhs = r.transpose(0, 2, 1, 3).reshape(norb * nva, kl * nvirt)
    wt = crossed_coupling.T
    ncol = wt.shape[0]
    core = lax.axis_index("core")
    out = jnp.zeros((lhs.shape[0], 2 * nchip, ncol), jnp.float32)
    for block, origin, _ in relay(wt, nchip):
        other = lax.ppermute(block, "core", [(0, 1), (1, 0)])
        for b, c in ((block, core), (other, 1 - core)):
            part = jnp.einsum("ak,nk->an", lhs, b, preferred_element_type=jnp.float32)
            at = 2 * origin + c
            cur = lax.dynamic_slice_in_dim(out, at, 1, axis=1)
            out = lax.dynamic_update_slice_in_dim(out, cur + part[:, None], at, axis=1)
    return out.reshape(nvirt, -1, nvirt)


def on_device_body(amplitudes, factors, crossed_amplitudes, crossed_coupling):
    nvirt = NV
    norb = lax.axis_size("orb")
    nchip = lax.axis_size("zz")
    t = lax.all_gather(amplitudes[0], "orb", axis=0, tiled=False)
    t, crossed_amplitudes = lax.optimization_barrier((t, crossed_amplitudes))
    ladder = ladder_term(t, factors, nvirt)
    crossed = crossed_term(crossed_amplitudes, crossed_coupling, nvirt, norb, nchip)
    total = (ladder + crossed).reshape((norb, nvirt // norb) + ladder.shape[1:])
    return reduce_scatter(total, norb)[None]


def reduce_scatter(total, norb):
    me = lax.axis_index("orb")
    acc = lax.dynamic_index_in_dim(total, me, axis=0, keepdims=False)
    pow2 = norb & (norb - 1) == 0
    for s in range(1, norb):
        if pow2:
            pairs = [(o, o ^ s) for o in range(norb)]
            dest = jnp.bitwise_xor(me, s)
        else:
            pairs = [(o, (o + s) % norb) for o in range(norb)]
            dest = (me + s) % norb
        blk = lax.dynamic_index_in_dim(total, dest, axis=0, keepdims=False)
        acc = acc + lax.ppermute(blk, "orb", pairs)
    return acc


def solution(mesh):
    npair, norb = mesh.shape["pair"], mesh.shape["orb"]
    sub = Mesh(mesh.devices.reshape(npair // 2, 2, norb), ("zz", "core", "orb"))
    return jax.shard_map(
        on_device_body,
        mesh=sub,
        in_specs=(
            P(PAIR, None, "orb", None),
            P("orb", PAIR),
            P(PAIR, None, "orb", None),
            P("orb", PAIR),
        ),
        out_specs=P(PAIR, "orb", None, None),
        check_vma=False,
    )
```

```python
import jax
import jax.numpy as jnp
from jax import lax
from jax.sharding import Mesh, PartitionSpec as P

NV = 600
PAIR = ("zz", "core")


def relay(x, n):
    zz = lax.axis_index("zz")
    out = [(x, zz, zz >= 0)]
    right, left = x, x
    for s in range(1, n):
        right = lax.ppermute(right, "zz", [(i, i + 1) for i in range(s - 1, n - 1)])
        left = lax.ppermute(left, "zz", [(j, j - 1) for j in range(1, n - s + 1)])
        out.append((right, jnp.maximum(zz - s, 0), zz - s >= 0))
        out.append((left, jnp.minimum(zz + s, n - 1), zz + s <= n - 1))
    return out


def relay_gather(x, n):
    core = lax.axis_index("core")
    buf = jnp.zeros((2 * n + 1,) + x.shape, x.dtype)
    for block, origin, valid in relay(x, n):
        other = lax.ppermute(block, "core", [(0, 1), (1, 0)])
        for b, c in ((block, core), (other, 1 - core)):
            at = jnp.where(valid, 2 * origin + c, 2 * n)
            buf = lax.dynamic_update_index_in_dim(buf, b, at, axis=0)
    return buf[: 2 * n]


def ladder_term(t, factors, nvirt):
    nj = t.shape[1]
    nq, cols = factors.shape
    if cols % nvirt == 0:
        g = relay_gather(factors.reshape(nq, cols // nvirt, nvirt), lax.axis_size("zz"))
        cube = None
    else:
        g = lax.all_gather(factors, PAIR, axis=0, tiled=False)
        cube = g.transpose(1, 0, 2).reshape(nq, nvirt, nvirt)
    return ladder_math(t, g, cube, nj, nvirt)


def ladder_math(t, g, cube, nj, nvirt):
    parts = []
    for j in range(nj):
        tj = t[:, j].reshape(nvirt, nvirt)
        if cube is None:
            inner = jnp.einsum("pqac,cd->pqad", g, tj, preferred_element_type=jnp.float32).astype(jnp.bfloat16)
            lj = jnp.einsum("pqad,rqbd->parb", inner, g, preferred_element_type=jnp.float32)
        else:
            inner = jnp.einsum("qac,cd->qad", cube, tj, preferred_element_type=jnp.float32).astype(jnp.bfloat16)
            lj = jnp.einsum("qad,qbd->ab", inner, cube, preferred_element_type=jnp.float32)
        parts.append(lj.reshape(nvirt, nvirt))
    return jnp.stack(parts, axis=1)


def crossed_term(crossed_amplitudes, crossed_coupling, nvirt, norb, nchip):
    ca = crossed_amplitudes[0]
    kocc, nva = ca.shape[0], ca.shape[1]
    kl = kocc // norb
    ca = ca.reshape(norb, kl, nva, nvirt)
    r = orb_exchange(ca, norb)
    lhs = r.transpose(0, 2, 1, 3).reshape(norb * nva, kl * nvirt)
    wt = crossed_coupling.T
    ncol = wt.shape[0]
    core = lax.axis_index("core")
    out = jnp.zeros((lhs.shape[0], 2 * nchip, ncol), jnp.float32)
    for block, origin, _ in relay(wt, nchip):
        other = lax.ppermute(block, "core", [(0, 1), (1, 0)])
        for b, c in ((block, core), (other, 1 - core)):
            part = jnp.einsum("ak,nk->an", lhs, b, preferred_element_type=jnp.float32)
            at = 2 * origin + c
            cur = lax.dynamic_slice_in_dim(out, at, 1, axis=1)
            out = lax.dynamic_update_slice_in_dim(out, cur + part[:, None], at, axis=1)
    return out.reshape(nvirt, -1, nvirt)


def on_device_body(amplitudes, factors, crossed_amplitudes, crossed_coupling):
    nvirt = NV
    norb = lax.axis_size("orb")
    nchip = lax.axis_size("zz")
    t = orb_gather(amplitudes[0], norb)
    t, crossed_amplitudes = lax.optimization_barrier((t, crossed_amplitudes))
    ladder = ladder_term(t, factors, nvirt)
    crossed = crossed_term(crossed_amplitudes, crossed_coupling, nvirt, norb, nchip)
    total = (ladder + crossed).reshape((norb, nvirt // norb) + ladder.shape[1:])
    return reduce_scatter(total, norb)[None]


def orb_gather(x, norb):
    me = lax.axis_index("orb")
    buf = jnp.zeros((norb,) + x.shape, x.dtype)
    buf = lax.dynamic_update_index_in_dim(buf, x, me, axis=0)
    pow2 = norb & (norb - 1) == 0
    for s in range(1, norb):
        if pow2:
            pairs = [(o, o ^ s) for o in range(norb)]
            src = jnp.bitwise_xor(me, s)
        else:
            pairs = [(o, (o + s) % norb) for o in range(norb)]
            src = (me - s) % norb
        buf = lax.dynamic_update_index_in_dim(buf, lax.ppermute(x, "orb", pairs), src, axis=0)
    return buf


def orb_exchange(x, norb):
    me = lax.axis_index("orb")
    buf = jnp.zeros(x.shape, x.dtype)
    own = lax.dynamic_index_in_dim(x, me, axis=0, keepdims=True)
    buf = lax.dynamic_update_slice_in_dim(buf, own, me, axis=0)
    pow2 = norb & (norb - 1) == 0
    for s in range(1, norb):
        if pow2:
            pairs = [(o, o ^ s) for o in range(norb)]
            dest = src = jnp.bitwise_xor(me, s)
        else:
            pairs = [(o, (o + s) % norb) for o in range(norb)]
            dest, src = (me + s) % norb, (me - s) % norb
        blk = lax.dynamic_index_in_dim(x, dest, axis=0, keepdims=True)
        buf = lax.dynamic_update_slice_in_dim(buf, lax.ppermute(blk, "orb", pairs), src, axis=0)
    return buf


def reduce_scatter(total, norb):
    me = lax.axis_index("orb")
    acc = lax.dynamic_index_in_dim(total, me, axis=0, keepdims=False)
    pow2 = norb & (norb - 1) == 0
    for s in range(1, norb):
        if pow2:
            pairs = [(o, o ^ s) for o in range(norb)]
            dest = jnp.bitwise_xor(me, s)
        else:
            pairs = [(o, (o + s) % norb) for o in range(norb)]
            dest = (me + s) % norb
        blk = lax.dynamic_index_in_dim(total, dest, axis=0, keepdims=False)
        acc = acc + lax.ppermute(blk, "orb", pairs)
    return acc


def solution(mesh):
    npair, norb = mesh.shape["pair"], mesh.shape["orb"]
    sub = Mesh(mesh.devices.reshape(npair // 2, 2, norb), ("zz", "core", "orb"))
    return jax.shard_map(
        on_device_body,
        mesh=sub,
        in_specs=(
            P(PAIR, None, "orb", None),
            P("orb", PAIR),
            P(PAIR, None, "orb", None),
            P("orb", PAIR),
        ),
        out_specs=P(PAIR, "orb", None, None),
        check_vma=False,
    )
```

```python
import jax
import jax.numpy as jnp
from jax import lax
from jax.sharding import Mesh, PartitionSpec as P

NV = 600
PAIR = ("zz", "core")


def relay(x, n):
    zz = lax.axis_index("zz")
    out = [(x, zz, zz >= 0)]
    right, left = x, x
    for s in range(1, n):
        right = lax.ppermute(right, "zz", [(i, i + 1) for i in range(s - 1, n - 1)])
        left = lax.ppermute(left, "zz", [(j, j - 1) for j in range(1, n - s + 1)])
        out.append((right, jnp.maximum(zz - s, 0), zz - s >= 0))
        out.append((left, jnp.minimum(zz + s, n - 1), zz + s <= n - 1))
    return out


def relay_gather(x, n):
    core = lax.axis_index("core")
    buf = jnp.zeros((2 * n + 1,) + x.shape, x.dtype)
    for block, origin, valid in relay(x, n):
        other = lax.ppermute(block, "core", [(0, 1), (1, 0)])
        for b, c in ((block, core), (other, 1 - core)):
            at = jnp.where(valid, 2 * origin + c, 2 * n)
            buf = lax.dynamic_update_index_in_dim(buf, b, at, axis=0)
    return buf[: 2 * n]


def ladder_term(t, factors, nvirt):
    nj = t.shape[1]
    nq, cols = factors.shape
    if cols % nvirt == 0:
        g = relay_gather(factors.reshape(nq, cols // nvirt, nvirt), lax.axis_size("zz"))
        cube = None
    else:
        g = lax.all_gather(factors, PAIR, axis=0, tiled=False)
        cube = g.transpose(1, 0, 2).reshape(nq, nvirt, nvirt)
    return ladder_math(t, g, cube, nj, nvirt)


def ladder_math(t, g, cube, nj, nvirt):
    parts = []
    for j in range(nj):
        tj = t[:, j].reshape(nvirt, nvirt)
        if cube is None:
            inner = jnp.einsum("pqac,cd->pqad", g, tj, preferred_element_type=jnp.float32).astype(jnp.bfloat16)
            lj = jnp.einsum("pqad,rqbd->parb", inner, g, preferred_element_type=jnp.float32)
        else:
            inner = jnp.einsum("qac,cd->qad", cube, tj, preferred_element_type=jnp.float32).astype(jnp.bfloat16)
            lj = jnp.einsum("qad,qbd->ab", inner, cube, preferred_element_type=jnp.float32)
        parts.append(lj.reshape(nvirt, nvirt))
    return jnp.stack(parts, axis=1)


def crossed_term(crossed_amplitudes, crossed_coupling, nvirt, norb, nchip):
    ca = crossed_amplitudes[0]
    kocc, nva = ca.shape[0], ca.shape[1]
    kl = kocc // norb
    ca = ca.reshape(norb, kl, nva, nvirt)
    r = lax.all_to_all(ca, "orb", 0, 0, tiled=True)
    lhs = r.transpose(0, 2, 1, 3).reshape(norb * nva, kl * nvirt)
    wt = crossed_coupling.T
    ncol = wt.shape[0]
    core = lax.axis_index("core")
    out = jnp.zeros((lhs.shape[0], 2 * nchip, ncol), jnp.float32)
    for block, origin, _ in relay(wt, nchip):
        other = lax.ppermute(block, "core", [(0, 1), (1, 0)])
        for b, c in ((block, core), (other, 1 - core)):
            part = jnp.einsum("ak,nk->an", lhs, b, preferred_element_type=jnp.float32)
            at = 2 * origin + c
            cur = lax.dynamic_slice_in_dim(out, at, 1, axis=1)
            out = lax.dynamic_update_slice_in_dim(out, cur + part[:, None], at, axis=1)
    return out.reshape(nvirt, -1, nvirt)


def on_device_body(amplitudes, factors, crossed_amplitudes, crossed_coupling):
    nvirt = NV
    norb = lax.axis_size("orb")
    nchip = lax.axis_size("zz")
    t = orb_gather(amplitudes[0], norb)
    t, crossed_amplitudes = lax.optimization_barrier((t, crossed_amplitudes))
    ladder = ladder_term(t, factors, nvirt)
    crossed = crossed_term(crossed_amplitudes, crossed_coupling, nvirt, norb, nchip)
    total = (ladder + crossed).reshape((norb, nvirt // norb) + ladder.shape[1:])
    return reduce_scatter(total, norb)[None]


def orb_gather(x, norb):
    me = lax.axis_index("orb")
    buf = jnp.zeros((norb,) + x.shape, x.dtype)
    buf = lax.dynamic_update_index_in_dim(buf, x, me, axis=0)
    pow2 = norb & (norb - 1) == 0
    for s in range(1, norb):
        if pow2:
            pairs = [(o, o ^ s) for o in range(norb)]
            src = jnp.bitwise_xor(me, s)
        else:
            pairs = [(o, (o + s) % norb) for o in range(norb)]
            src = (me - s) % norb
        buf = lax.dynamic_update_index_in_dim(buf, lax.ppermute(x, "orb", pairs), src, axis=0)
    return buf


def reduce_scatter(total, norb):
    me = lax.axis_index("orb")
    acc = lax.dynamic_index_in_dim(total, me, axis=0, keepdims=False)
    pow2 = norb & (norb - 1) == 0
    for s in range(1, norb):
        if pow2:
            pairs = [(o, o ^ s) for o in range(norb)]
            dest = jnp.bitwise_xor(me, s)
        else:
            pairs = [(o, (o + s) % norb) for o in range(norb)]
            dest = (me + s) % norb
        blk = lax.dynamic_index_in_dim(total, dest, axis=0, keepdims=False)
        acc = acc + lax.ppermute(blk, "orb", pairs)
    return acc


def solution(mesh):
    npair, norb = mesh.shape["pair"], mesh.shape["orb"]
    sub = Mesh(mesh.devices.reshape(npair // 2, 2, norb), ("zz", "core", "orb"))
    return jax.shard_map(
        on_device_body,
        mesh=sub,
        in_specs=(
            P(PAIR, None, "orb", None),
            P("orb", PAIR),
            P(PAIR, None, "orb", None),
            P("orb", PAIR),
        ),
        out_specs=P(PAIR, "orb", None, None),
        check_vma=False,
    )
```
